512 devices in a mesh: band: 128 (over x, z_hi, y, core), depth: 4 (over z_lo).
Axes of the slice: x: 4, y: 8, z: 8 (z_hi: 2, z_lo: 4; z = z_hi * 4 + z_lo), core: 2. Of those that a mesh axis runs over, the one named last changes fastest.
Arguments:
- orbitals: bfloat16 [128, 32, 128, 128], P('band', 'depth'), may hold values from -6 to 6
- dielectric: float32 [32, 128, 128], P('depth'), may hold values from 1 to 4
- occupied: int32 [128], P('band'), may hold values 0 or 1
- plan: int32 [2, 128, 1], P(None, 'band'), may hold values 0 or 1
Outputs:
- exchange: float32 [128, 32, 128, 128], P('band', 'depth')
The draws below stay inside these ranges and needn't reach their ends.
All inputs are finite; a program needn't handle non-finite values. No bound on the sum of `occupied` or of `plan` on one device may be relied on, other than what follows from the above.
Results may differ from the reference program's by a relative error of at most 0.0003.
Values may be sent and summed in bfloat16 or wider, within the bound.
No kernel may reach another device: no remote copies, remote signals or barrier semaphores. Data moves between devices by JAX's collectives and lax.ppermute only.
A program may use at most 64 MiB of HBM per device.

```python
import math
import jax
import jax.numpy as jnp
from jax import lax

BD = 1
NX = 128
NY = 128
NZ = 32
TICKS = 2
SWEEPS = 2
NB = 128


def place_ends(result, key, least, high):
    longest = result.shape.index(max(result.shape))
    spots = []
    for shift in (0, 1):
        where = [jax.random.randint(jax.random.fold_in(key, axis), (), 0, length) for axis, length in enumerate(result.shape)]
        where[longest] = (where[longest] + shift) % result.shape[longest]
        spots.append(tuple(where))
    return result.at[spots[0]].set(least).at[spots[1]].set(high)


def level_of(own_key, extent, split, low, top_value):
    def one(axis_at, shards_of):
        steps = jax.random.uniform(jax.random.fold_in(jax.random.fold_in(own_key, 6), axis_at), (shards_of,), jnp.float32, low / len(split), top_value / len(split))
        return jnp.repeat(jnp.exp(steps), extent[axis_at] // shards_of).reshape((-1,) + (1,) * (len(extent) - axis_at - 1))

    gain = one(*split[0])
    for cut in split[1:]:
        gain = gain * one(*cut)
    return gain


def gaussian(rng, dims, spread, reach, pieces=(), dtype=jnp.bfloat16):
    gain = level_of(rng, dims, pieces, -0.22, 0.18) if pieces else 1.0
    array = jax.random.normal(rng, dims, jnp.float32) * spread * gain
    return jnp.minimum(jnp.maximum(array, -reach), reach).astype(dtype)


def setup_inputs(seed: int = 0) -> dict:
    splits = jax.random.split(jax.random.key(seed), 5)
    return {
        "orbitals": gaussian(splits[0], (NB, NZ, NX, NY), 1.0, 6.0, ((0, 128), (1, 4))),
        "dielectric": jnp.clip(jnp.exp(math.log(4.0) - 1.3862944 * jax.random.uniform(splits[1], (NZ, NX, NY), jnp.float32) ** level_of(splits[1], (NZ, NX, NY), ((0, 4),), -0.2, 0.2)), 1.0, 4.0),
        "occupied": place_ends((jax.random.randint(splits[2], (NB,), 0, 4) < 3).astype(jnp.int32), jax.random.fold_in(splits[2], 1), 0, 1),
        "plan": place_ends((jax.random.randint(splits[3], (TICKS, NB, BD), 0, 4) < 3).astype(jnp.int32), jax.random.fold_in(splits[3], 1), 0, 1),
    }


FOUR_PI = 4.0 * math.pi
KAPPA_SQ = 4.0
CHEB_CENTER = 28.0
CHEB_HALF = 24.0


def face_tables(dielectric):
    face_z = (dielectric + jnp.roll(dielectric, -1, 0)) * 0.5
    face_x = (dielectric + jnp.roll(dielectric, -1, 1)) * 0.5
    face_y = (dielectric + jnp.roll(dielectric, -1, 2)) * 0.5
    return face_z, face_x, face_y


def operator_apply(field, faces):
    face_z, face_x, face_y = faces
    flux_z = face_z * (jnp.roll(field, -1, -3) - field)
    part_z = flux_z - jnp.roll(flux_z, 1, -3)
    flux_x = face_x * (jnp.roll(field, -1, -2) - field)
    part_x = flux_x - jnp.roll(flux_x, 1, -2)
    flux_y = face_y * (jnp.roll(field, -1, -1) - field)
    part_y = flux_y - jnp.roll(flux_y, 1, -1)
    return KAPPA_SQ * field - (part_z + part_x + part_y)


def chebyshev(source, faces):
    sigma = CHEB_CENTER / CHEB_HALF
    direction = source / CHEB_CENTER
    solution = direction
    remainder = source
    factor = CHEB_HALF / CHEB_CENTER
    for sweep in range(SWEEPS):
        remainder = remainder - operator_apply(direction, faces)
        factor_next = 1.0 / (2.0 * sigma - factor)
        direction = (factor_next * factor) * direction + (2.0 * factor_next / CHEB_HALF) * remainder
        solution = solution + direction
        factor = factor_next
    return solution


def reference(orbitals, dielectric, occupied, plan):
    blocks = NB // BD
    faces = face_tables(dielectric)
    psi_blocks = orbitals.reshape(blocks, BD, NZ, NX, NY)
    occ_blocks = occupied.astype(jnp.float32).reshape(blocks, BD)
    weights = plan.astype(jnp.float32).reshape(TICKS, blocks, BD, BD)
    totals = jnp.zeros((blocks, BD, NZ, NX, NY), jnp.float32)
    for tick in range(TICKS):
        partner_psi = jnp.roll(psi_blocks, tick + 1, 0)
        partner_occ = jnp.roll(occ_blocks, tick + 1, 0)

        def one_block(items):
            own_psi, far_psi, own_occ, far_occ, pair_flags = items
            own_wide = own_psi.astype(jnp.float32)
            far_wide = far_psi.astype(jnp.float32)
            density = FOUR_PI * own_wide[:, None] * far_wide[None, :]
            potential = chebyshev(density, faces)
            coef_own = pair_flags * far_occ[None, :]
            mine = jnp.sum(coef_own[:, :, None, None, None] * potential * far_wide[None, :], axis=1)
            coef_back = pair_flags * own_occ[:, None]
            theirs = jnp.sum(coef_back[:, :, None, None, None] * potential * own_wide[:, None], axis=0)
            return mine, theirs

        mine, theirs = lax.map(one_block, (psi_blocks, partner_psi, occ_blocks, partner_occ, weights[tick]))
        totals = totals + mine + jnp.roll(theirs, -(tick + 1), 0)
    return (-totals).reshape(NB, NZ, NX, NY)
```

```python
import math

import jax
import jax.numpy as jnp
from jax import lax
from jax.sharding import PartitionSpec as P

SWEEPS = 2


FOUR_PI = 4.0 * math.pi
KAPPA_SQ = 4.0
CHEB_CENTER = 28.0
CHEB_HALF = 24.0
HALO = SWEEPS


def shifted(x, axis, by):
    size = lax.axis_size(axis)
    return lax.ppermute(x, axis, [(i, (i + by) % size) for i in range(size)])


def z_halo(x, dim, width):
    length = x.shape[dim]
    last = lax.slice_in_dim(x, length - width, length, axis=dim)
    leading = lax.slice_in_dim(x, 0, width, axis=dim)
    before = shifted(last, "depth", 1)
    after = shifted(leading, "depth", -1)
    return jnp.concatenate([before, x, after], axis=dim)


def stencil(field, coef_z, coef_x, coef_y):
    flux_z = coef_z * (field[..., 1:, :, :] - field[..., :-1, :, :])
    part_z = flux_z[..., 1:, :, :] - flux_z[..., :-1, :, :]
    center = field[..., 1:-1, :, :]
    flux_x = coef_x * (jnp.roll(center, -1, -2) - center)
    part_x = flux_x - jnp.roll(flux_x, 1, -2)
    flux_y = coef_y * (jnp.roll(center, -1, -1) - center)
    part_y = flux_y - jnp.roll(flux_y, 1, -1)
    return KAPPA_SQ * center - (part_z + part_x + part_y)


def potential_of(source, face_z, face_x, face_y):
    sigma = CHEB_CENTER / CHEB_HALF
    factor = CHEB_HALF / CHEB_CENTER
    direction = source / CHEB_CENTER
    solution = direction
    remainder = source
    lo = 0
    for sweep in range(SWEEPS):
        n = direction.shape[-3]
        applied = stencil(
            direction,
            face_z[lo : lo + n - 1],
            face_x[lo + 1 : lo + n - 1],
            face_y[lo + 1 : lo + n - 1],
        )
        lo += 1
        remainder = remainder[..., 1:-1, :, :] - applied
        factor_next = 1.0 / (2.0 * sigma - factor)
        direction = factor_next * factor * direction[..., 1:-1, :, :] + 2.0 * factor_next / CHEB_HALF * remainder
        solution = solution[..., 1:-1, :, :] + direction
        factor = factor_next
    return solution


def on_device(orbitals, dielectric, occupied, plan):
    psi = orbitals[0]
    occ = occupied.astype(jnp.bfloat16)[0]
    flags = plan.astype(jnp.bfloat16).reshape(plan.shape[0])

    padded_diel = z_halo(dielectric, 0, HALO)
    face_z = (padded_diel[:-1] + padded_diel[1:]) * 0.5
    face_x = (padded_diel + jnp.roll(padded_diel, -1, 1)) * 0.5
    face_y = (padded_diel + jnp.roll(padded_diel, -1, 2)) * 0.5

    ticks = plan.shape[0]
    lower = psi * occ
    slabs = [psi]
    for tick in range(1, ticks + 1):
        slabs.append(shifted(lower, "band", tick))
    for tick in range(1, ticks + 1):
        slabs.append(shifted(psi * (flags[tick - 1] * occ), "band", -tick))
    stack = jnp.stack(slabs)
    wide = z_halo(stack, 1, HALO).astype(jnp.float32)
    own = wide[0]
    partners = wide[1:]
    density = (FOUR_PI * own)[None] * partners
    potential = potential_of(density, face_z, face_x, face_y)
    weights = jnp.concatenate(
        [plan.astype(jnp.float32).reshape(ticks), jnp.ones((ticks,), jnp.float32)]
    )
    terms = weights[:, None, None, None] * potential * partners[:, HALO:-HALO]
    totals = jnp.sum(terms, axis=0)
    return -totals[None]


def solution(mesh):
    placed = (
        P("band", "depth", None, None),
        P("depth", None, None),
        P("band"),
        P(None, "band", None),
    )
    return jax.shard_map(
        on_device,
        mesh=mesh,
        in_specs=placed,
        out_specs=P("band", "depth", None, None),
        check_vma=False,
    )
```

```python
import math

import jax
import jax.numpy as jnp
from jax import lax
from jax.experimental import pallas as pl
from jax.experimental.pallas import tpu as pltpu
from jax.sharding import PartitionSpec as P

SWEEPS = 2


FOUR_PI = 4.0 * math.pi
KAPPA_SQ = 4.0
CHEB_CENTER = 28.0
CHEB_HALF = 24.0
HALO = SWEEPS


def shifted(x, axis, by):
    size = lax.axis_size(axis)
    return lax.ppermute(x, axis, [(i, (i + by) % size) for i in range(size)])


def z_halo(x, dim, width):
    length = x.shape[dim]
    last = lax.slice_in_dim(x, length - width, length, axis=dim)
    leading = lax.slice_in_dim(x, 0, width, axis=dim)
    before = shifted(last, "depth", 1)
    after = shifted(leading, "depth", -1)
    return jnp.concatenate([before, x, after], axis=dim)


def solve_kernel(weight_ref, psi_ref, eps_ref, out_ref, face_z, face_x, face_y, dens, first, rem, second, partial):
    layers, rows, cols = eps_ref.shape
    pairs = psi_ref.shape[0] - 1

    def faces(e, carry):
        cur = eps_ref[e]
        face_x[e] = (cur + pltpu.roll(cur, rows - 1, 0)) * 0.5
        face_y[e] = (cur + pltpu.roll(cur, cols - 1, 1)) * 0.5
        return carry

    lax.fori_loop(0, layers, faces, 0)

    def faces_z(e, carry):
        face_z[e] = (eps_ref[e] + eps_ref[e + 1]) * 0.5
        return carry

    lax.fori_loop(0, layers - 1, faces_z, 0)

    def applied(field, e):
        center = field[e]
        flux_up = face_z[e] * (field[e + 1] - center)
        flux_down = face_z[e - 1] * (center - field[e - 1])
        part_z = flux_up - flux_down
        flux_x = face_x[e] * (pltpu.roll(center, rows - 1, 0) - center)
        part_x = flux_x - pltpu.roll(flux_x, 1, 0)
        flux_y = face_y[e] * (pltpu.roll(center, cols - 1, 1) - center)
        part_y = flux_y - pltpu.roll(flux_y, 1, 1)
        return KAPPA_SQ * center - (part_z + part_x + part_y)

    sigma = CHEB_CENTER / CHEB_HALF
    factor = CHEB_HALF / CHEB_CENTER
    factor_one = 1.0 / (2.0 * sigma - factor)
    factor_two = 1.0 / (2.0 * sigma - factor_one)
    keep_one, mix_one = factor_one * factor, 2.0 * factor_one / CHEB_HALF
    keep_two, mix_two = factor_two * factor_one, 2.0 * factor_two / CHEB_HALF

    out_ref[...] = jnp.zeros(out_ref.shape, out_ref.dtype)
    for k in range(pairs):
        weight = weight_ref[k]

        def density(e, carry):
            own = psi_ref[0, e].astype(jnp.float32)
            partner = psi_ref[k + 1, e].astype(jnp.float32)
            value = (FOUR_PI * own) * partner
            dens[e] = value
            first[e] = value / CHEB_CENTER
            return carry

        lax.fori_loop(0, layers, density, 0)

        def sweep_one(e, carry):
            center = first[e]
            remainder = dens[e] - applied(first, e)
            direction = keep_one * center + mix_one * remainder
            rem[e] = remainder
            second[e] = direction
            partial[e] = center + direction
            return carry

        lax.fori_loop(1, layers - 1, sweep_one, 0)

        def sweep_two(e, carry):
            remainder = rem[e] - applied(second, e)
            direction = keep_two * second[e] + mix_two * remainder
            potential = partial[e] + direction
            partner = psi_ref[k + 1, e].astype(jnp.float32)
            out_ref[e - HALO] += (weight * potential) * partner
            return carry

        lax.fori_loop(HALO, layers - HALO, sweep_two, 0)
    out_ref[...] = -out_ref[...]


def solve(weights, wide, padded_diel):
    layers, rows, cols = padded_diel.shape
    pairs = wide.shape[0] - 1
    full = jax.ShapeDtypeStruct((layers, rows, cols), jnp.float32)
    vmem = pltpu.VMEM
    return pl.pallas_call(
        solve_kernel,
        out_shape=jax.ShapeDtypeStruct((layers - 2 * HALO, rows, cols), jnp.float32),
        in_specs=[
            pl.BlockSpec(memory_space=pltpu.SMEM),
            pl.BlockSpec(memory_space=vmem),
            pl.BlockSpec(memory_space=vmem),
        ],
        out_specs=pl.BlockSpec(memory_space=vmem),
        scratch_shapes=[vmem((layers - 1, rows, cols), jnp.float32)] + [vmem(full.shape, jnp.float32)] * 7,
        compiler_params=pltpu.CompilerParams(vmem_limit_bytes=48 * 1024 * 1024),
        cost_estimate=pl.CostEstimate(
            flops=pairs * 3 * layers * rows * cols * 30,
            transcendentals=0,
            bytes_accessed=wide.size * 2 + padded_diel.size * 4 + (layers - 2 * HALO) * rows * cols * 4,
        ),
    )(weights, wide, padded_diel)


def on_device(orbitals, dielectric, occupied, plan):
    psi = orbitals[0]
    occ = occupied.astype(jnp.bfloat16)[0]
    flags = plan.astype(jnp.bfloat16).reshape(plan.shape[0])
    padded_diel = z_halo(dielectric, 0, HALO)

    ticks = plan.shape[0]
    lower = psi * occ
    slabs = [psi]
    for tick in range(1, ticks + 1):
        slabs.append(shifted(lower, "band", tick))
    for tick in range(1, ticks + 1):
        slabs.append(shifted(psi * (flags[tick - 1] * occ), "band", -tick))
    wide = z_halo(jnp.stack(slabs), 1, HALO)
    weights = jnp.concatenate(
        [plan.astype(jnp.float32).reshape(ticks), jnp.ones((ticks,), jnp.float32)]
    )
    return solve(weights, wide, padded_diel)[None]


def solution(mesh):
    placed = (
        P("band", "depth", None, None),
        P("depth", None, None),
        P("band"),
        P(None, "band", None),
    )
    return jax.shard_map(
        on_device,
        mesh=mesh,
        in_specs=placed,
        out_specs=P("band", "depth", None, None),
        check_vma=False,
    )
```

```python
import math

import jax
import jax.numpy as jnp
from jax import lax
from jax.experimental import pallas as pl
from jax.experimental.pallas import tpu as pltpu
from jax.sharding import PartitionSpec as P

SWEEPS = 2


FOUR_PI = 4.0 * math.pi
KAPPA_SQ = 4.0
CHEB_CENTER = 28.0
CHEB_HALF = 24.0
HALO = SWEEPS


def shifted(x, axis, by):
    size = lax.axis_size(axis)
    return lax.ppermute(x, axis, [(i, (i + by) % size) for i in range(size)])


def z_halo(x, dim, width):
    length = x.shape[dim]
    last = lax.slice_in_dim(x, length - width, length, axis=dim)
    leading = lax.slice_in_dim(x, 0, width, axis=dim)
    before = shifted(last, "depth", 1)
    after = shifted(leading, "depth", -1)
    return jnp.concatenate([before, x, after], axis=dim)


def solve_kernel(weight_ref, psi_ref, eps_ref, out_ref, face_z, face_x, face_y, dens, first, rem, second, partial):
    layers, rows, cols = eps_ref.shape
    pairs = psi_ref.shape[0] - 1

    def faces(e, carry):
        cur = eps_ref[e]
        face_x[e] = (cur + pltpu.roll(cur, rows - 1, 0)) * 0.5
        face_y[e] = (cur + pltpu.roll(cur, cols - 1, 1)) * 0.5
        return carry

    lax.fori_loop(0, layers, faces, 0)

    def faces_z(e, carry):
        face_z[e] = (eps_ref[e] + eps_ref[e + 1]) * 0.5
        return carry

    lax.fori_loop(0, layers - 1, faces_z, 0)

    def applied(field, e):
        center = field[e]
        flux_up = face_z[e] * (field[e + 1] - center)
        flux_down = face_z[e - 1] * (center - field[e - 1])
        part_z = flux_up - flux_down
        flux_x = face_x[e] * (pltpu.roll(center, rows - 1, 0) - center)
        part_x = flux_x - pltpu.roll(flux_x, 1, 0)
        flux_y = face_y[e] * (pltpu.roll(center, cols - 1, 1) - center)
        part_y = flux_y - pltpu.roll(flux_y, 1, 1)
        return KAPPA_SQ * center - (part_z + part_x + part_y)

    sigma = CHEB_CENTER / CHEB_HALF
    factor = CHEB_HALF / CHEB_CENTER
    factor_one = 1.0 / (2.0 * sigma - factor)
    factor_two = 1.0 / (2.0 * sigma - factor_one)
    keep_one, mix_one = factor_one * factor, 2.0 * factor_one / CHEB_HALF
    keep_two, mix_two = factor_two * factor_one, 2.0 * factor_two / CHEB_HALF

    out_ref[...] = jnp.zeros(out_ref.shape, out_ref.dtype)
    for k in range(pairs):
        weight = weight_ref[k]

        def density(e, carry):
            own = psi_ref[0, e].astype(jnp.float32)
            partner = psi_ref[k + 1, e].astype(jnp.float32)
            value = (FOUR_PI * own) * partner
            dens[e] = value
            first[e] = value / CHEB_CENTER
            return carry

        lax.fori_loop(0, layers, density, 0)

        def sweep_one(e, carry):
            center = first[e]
            remainder = dens[e] - applied(first, e)
            direction = keep_one * center + mix_one * remainder
            rem[e] = remainder
            second[e] = direction
            partial[e] = center + direction
            return carry

        lax.fori_loop(1, layers - 1, sweep_one, 0)

        def sweep_two(e, carry):
            remainder = rem[e] - applied(second, e)
            direction = keep_two * second[e] + mix_two * remainder
            potential = partial[e] + direction
            partner = psi_ref[k + 1, e].astype(jnp.float32)
            out_ref[e - HALO] += (weight * potential) * partner
            return carry

        lax.fori_loop(HALO, layers - HALO, sweep_two, 0)
    out_ref[...] = -out_ref[...]


def solve(weights, wide, padded_diel):
    layers, rows, cols = padded_diel.shape
    pairs = wide.shape[0] - 1
    full = jax.ShapeDtypeStruct((layers, rows, cols), jnp.float32)
    vmem = pltpu.VMEM
    return pl.pallas_call(
        solve_kernel,
        out_shape=jax.ShapeDtypeStruct((layers - 2 * HALO, rows, cols), jnp.float32),
        in_specs=[
            pl.BlockSpec(memory_space=pltpu.SMEM),
            pl.BlockSpec(memory_space=vmem),
            pl.BlockSpec(memory_space=vmem),
        ],
        out_specs=pl.BlockSpec(memory_space=vmem),
        scratch_shapes=[vmem((layers - 1, rows, cols), jnp.float32)] + [vmem(full.shape, jnp.float32)] * 7,
        compiler_params=pltpu.CompilerParams(vmem_limit_bytes=48 * 1024 * 1024),
        cost_estimate=pl.CostEstimate(
            flops=pairs * 3 * layers * rows * cols * 30,
            transcendentals=0,
            bytes_accessed=wide.size * 2 + padded_diel.size * 4 + (layers - 2 * HALO) * rows * cols * 4,
        ),
    )(weights, wide, padded_diel)


def exchanged(x, axis, pairs_of):
    size = lax.axis_size(axis)
    return lax.ppermute(x, axis, [(i, pairs_of(i) % size) for i in range(size)])


def on_device(orbitals, dielectric, occupied, plan):
    psi = orbitals[0]
    depth, rows, cols = psi.shape
    ticks = plan.shape[0]
    flags = plan.astype(jnp.float32).reshape(ticks)
    padded_diel = z_halo(dielectric, 0, HALO)

    info = jnp.zeros((16, cols), jnp.bfloat16).at[0, :ticks].set(plan.astype(jnp.bfloat16).reshape(ticks))
    message = jnp.concatenate(
        [(psi * occupied.astype(jnp.bfloat16)[0]).reshape(depth * rows, cols), info], axis=0
    )
    swap = exchanged(message, "band", lambda b: b ^ 1)
    outer = exchanged(message, "band", lambda b: b + 1 if b % 2 else b - 1)
    far = exchanged(message, "band", lambda b: b - 2 if b % 2 else b + 2)
    relay = exchanged(outer, "band", lambda b: b ^ 1)

    def slab(m):
        return m[: depth * rows].reshape(depth, rows, cols)

    def sent_flags(m):
        return m[depth * rows, :ticks].astype(jnp.float32)

    odd = lax.axis_index("band") % 2 == 1
    weights = jnp.stack(
        [
            jnp.where(odd, flags[0], sent_flags(swap)[0]),
            jnp.where(odd, sent_flags(outer)[0], flags[0]),
            jnp.where(odd, sent_flags(far)[1], flags[1]),
            jnp.where(odd, flags[1], sent_flags(relay)[1]),
        ]
    )
    stack = jnp.stack([psi, slab(swap), slab(outer), slab(far), slab(relay)])
    wide = z_halo(stack, 1, HALO)
    return solve(weights, wide, padded_diel)[None]


def solution(mesh):
    placed = (
        P("band", "depth", None, None),
        P("depth", None, None),
        P("band"),
        P(None, "band", None),
    )
    return jax.shard_map(
        on_device,
        mesh=mesh,
        in_specs=placed,
        out_specs=P("band", "depth", None, None),
        check_vma=False,
    )
```

```python
import math

import jax
import jax.numpy as jnp
from jax import lax
from jax.experimental import pallas as pl
from jax.experimental.pallas import tpu as pltpu
from jax.sharding import PartitionSpec as P

SWEEPS = 2


FOUR_PI = 4.0 * math.pi
KAPPA_SQ = 4.0
CHEB_CENTER = 28.0
CHEB_HALF = 24.0
HALO = SWEEPS


def shifted(x, axis, by):
    size = lax.axis_size(axis)
    return lax.ppermute(x, axis, [(i, (i + by) % size) for i in range(size)])


def z_halo(x, dim, width):
    length = x.shape[dim]
    last = lax.slice_in_dim(x, length - width, length, axis=dim)
    leading = lax.slice_in_dim(x, 0, width, axis=dim)
    before = shifted(last, "depth", 1)
    after = shifted(leading, "depth", -1)
    return jnp.concatenate([before, x, after], axis=dim)


def solve_kernel(weight_ref, psi_ref, eps_ref, out_ref, face_z, face_x, face_y, dens, first, rem, second, partial):
    layers, rows, cols = eps_ref.shape
    pairs = psi_ref.shape[0] - 1

    def faces(e, carry):
        cur = eps_ref[e]
        face_x[e] = (cur + pltpu.roll(cur, rows - 1, 0)) * 0.5
        face_y[e] = (cur + pltpu.roll(cur, cols - 1, 1)) * 0.5
        return carry

    lax.fori_loop(0, layers, faces, 0)

    def faces_z(e, carry):
        face_z[e] = (eps_ref[e] + eps_ref[e + 1]) * 0.5
        return carry

    lax.fori_loop(0, layers - 1, faces_z, 0)

    def applied(field, e):
        center = field[e]
        flux_up = face_z[e] * (field[e + 1] - center)
        flux_down = face_z[e - 1] * (center - field[e - 1])
        part_z = flux_up - flux_down
        flux_x = face_x[e] * (pltpu.roll(center, rows - 1, 0) - center)
        part_x = flux_x - pltpu.roll(flux_x, 1, 0)
        flux_y = face_y[e] * (pltpu.roll(center, cols - 1, 1) - center)
        part_y = flux_y - pltpu.roll(flux_y, 1, 1)
        return KAPPA_SQ * center - (part_z + part_x + part_y)

    sigma = CHEB_CENTER / CHEB_HALF
    factor = CHEB_HALF / CHEB_CENTER
    factor_one = 1.0 / (2.0 * sigma - factor)
    factor_two = 1.0 / (2.0 * sigma - factor_one)
    keep_one, mix_one = factor_one * factor, 2.0 * factor_one / CHEB_HALF
    keep_two, mix_two = factor_two * factor_one, 2.0 * factor_two / CHEB_HALF

    out_ref[...] = jnp.zeros(out_ref.shape, out_ref.dtype)
    for k in range(pairs):
        weight = weight_ref[k]

        def density(e, carry):
            own = psi_ref[0, e].astype(jnp.float32)
            partner = psi_ref[k + 1, e].astype(jnp.float32)
            value = (FOUR_PI * own) * partner
            dens[e] = value
            first[e] = value / CHEB_CENTER
            return carry

        lax.fori_loop(0, layers, density, 0)

        def sweep_one(e, carry):
            center = first[e]
            remainder = dens[e] - applied(first, e)
            direction = keep_one * center + mix_one * remainder
            rem[e] = remainder
            second[e] = direction
            partial[e] = center + direction
            return carry

        lax.fori_loop(1, layers - 1, sweep_one, 0)

        def sweep_two(e, carry):
            remainder = rem[e] - applied(second, e)
            direction = keep_two * second[e] + mix_two * remainder
            potential = partial[e] + direction
            partner = psi_ref[k + 1, e].astype(jnp.float32)
            out_ref[e - HALO] += (weight * potential) * partner
            return carry

        lax.fori_loop(HALO, layers - HALO, sweep_two, 0)
    out_ref[...] = -out_ref[...]


def solve(weights, wide, padded_diel):
    layers, rows, cols = padded_diel.shape
    pairs = wide.shape[0] - 1
    full = jax.ShapeDtypeStruct((layers, rows, cols), jnp.float32)
    vmem = pltpu.VMEM
    return pl.pallas_call(
        solve_kernel,
        out_shape=jax.ShapeDtypeStruct((layers - 2 * HALO, rows, cols), jnp.float32),
        in_specs=[
            pl.BlockSpec(memory_space=vmem),
            pl.BlockSpec(memory_space=vmem),
            pl.BlockSpec(memory_space=vmem),
        ],
        out_specs=pl.BlockSpec(memory_space=vmem),
        scratch_shapes=[vmem((layers - 1, rows, cols), jnp.float32)] + [vmem(full.shape, jnp.float32)] * 7,
        compiler_params=pltpu.CompilerParams(vmem_limit_bytes=48 * 1024 * 1024),
        cost_estimate=pl.CostEstimate(
            flops=pairs * 3 * layers * rows * cols * 30,
            transcendentals=0,
            bytes_accessed=wide.size * 2 + padded_diel.size * 4 + (layers - 2 * HALO) * rows * cols * 4,
        ),
    )(weights, wide, padded_diel)


def exchanged(x, axis, pairs_of):
    size = lax.axis_size(axis)
    return lax.ppermute(x, axis, [(i, pairs_of(i) % size) for i in range(size)])


def on_device(orbitals, dielectric, occupied, plan):
    psi = orbitals[0]
    depth, rows, cols = psi.shape
    ticks = plan.shape[0]
    flags = plan.astype(jnp.float32).reshape(ticks)
    padded_diel = z_halo(dielectric, 0, HALO)

    info = jnp.zeros((16, cols), jnp.bfloat16).at[:ticks, :].set(
        jnp.broadcast_to(plan.astype(jnp.bfloat16).reshape(ticks, 1), (ticks, cols))
    )
    message = jnp.concatenate(
        [(psi * occupied.astype(jnp.bfloat16)[0]).reshape(depth * rows, cols), info], axis=0
    )
    swap = exchanged(message, "band", lambda b: b ^ 1)
    outer = exchanged(message, "band", lambda b: b + 1 if b % 2 else b - 1)
    far = exchanged(message, "band", lambda b: b - 2 if b % 2 else b + 2)
    relay = exchanged(outer, "band", lambda b: b ^ 1)

    def slab(m):
        return m[: depth * rows].reshape(depth, rows, cols)

    def sent_flags(m, tick):
        return m[depth * rows + tick : depth * rows + tick + 1].astype(jnp.float32)

    def own_flags(tick):
        return jnp.broadcast_to(flags[tick], (1, cols))

    odd = lax.axis_index("band") % 2 == 1
    weights = jnp.stack(
        [
            jnp.where(odd, own_flags(0), sent_flags(swap, 0)),
            jnp.where(odd, sent_flags(outer, 0), own_flags(0)),
            jnp.where(odd, sent_flags(far, 1), own_flags(1)),
            jnp.where(odd, own_flags(1), sent_flags(relay, 1)),
        ]
    )
    stack = jnp.stack([psi, slab(swap), slab(outer), slab(far), slab(relay)])
    wide = z_halo(stack, 1, HALO)
    return solve(weights, wide, padded_diel)[None]


def solution(mesh):
    placed = (
        P("band", "depth", None, None),
        P("depth", None, None),
        P("band"),
        P(None, "band", None),
    )
    return jax.shard_map(
        on_device,
        mesh=mesh,
        in_specs=placed,
        out_specs=P("band", "depth", None, None),
        check_vma=False,
    )
```

```python
import functools
import math

import jax
import jax.numpy as jnp
from jax import lax
from jax.experimental import pallas as pl
from jax.experimental.pallas import tpu as pltpu
from jax.sharding import PartitionSpec as P

SWEEPS = 2


FOUR_PI = 4.0 * math.pi
KAPPA_SQ = 4.0
CHEB_CENTER = 28.0
CHEB_HALF = 24.0
HALO = SWEEPS


def shifted(x, axis, by):
    size = lax.axis_size(axis)
    return lax.ppermute(x, axis, [(i, (i + by) % size) for i in range(size)])


def z_halo(x, dim, width):
    length = x.shape[dim]
    last = lax.slice_in_dim(x, length - width, length, axis=dim)
    leading = lax.slice_in_dim(x, 0, width, axis=dim)
    before = shifted(last, "depth", 1)
    after = shifted(leading, "depth", -1)
    return jnp.concatenate([before, x, after], axis=dim)


def solve_kernel(windows, weight_ref, psi_ref, eps_ref, out_ref, face_z, face_x, face_y, dens, first, rem, second, partial, flux):
    _, rows, cols = eps_ref.shape
    pairs = psi_ref.shape[0] - 1

    def applied(field, e):
        center = field[e]
        flux_up = face_z[e] * (field[e + 1] - center)
        flux_down = flux[...]
        flux[...] = flux_up
        part_z = flux_up - flux_down
        flux_x = face_x[e] * (pltpu.roll(center, rows - 1, 0) - center)
        part_x = flux_x - pltpu.roll(flux_x, 1, 0)
        flux_y = face_y[e] * (pltpu.roll(center, cols - 1, 1) - center)
        part_y = flux_y - pltpu.roll(flux_y, 1, 1)
        return KAPPA_SQ * center - (part_z + part_x + part_y)

    sigma = CHEB_CENTER / CHEB_HALF
    factor = CHEB_HALF / CHEB_CENTER
    factor_one = 1.0 / (2.0 * sigma - factor)
    factor_two = 1.0 / (2.0 * sigma - factor_one)
    keep_one, mix_one = factor_one * factor, 2.0 * factor_one / CHEB_HALF
    keep_two, mix_two = factor_two * factor_one, 2.0 * factor_two / CHEB_HALF

    out_ref[...] = jnp.zeros(out_ref.shape, out_ref.dtype)
    out_at = 0
    for start, size in windows:

        def faces(e, carry):
            cur = eps_ref[start + e]
            face_x[e] = (cur + pltpu.roll(cur, rows - 1, 0)) * 0.5
            face_y[e] = (cur + pltpu.roll(cur, cols - 1, 1)) * 0.5
            face_z[e] = (cur + eps_ref[start + e + 1]) * 0.5
            return carry

        lax.fori_loop(0, size - 1, faces, 0)

        for k in range(pairs):
            weight = weight_ref[k]

            def density(e, carry):
                own = psi_ref[0, start + e].astype(jnp.float32)
                partner = psi_ref[k + 1, start + e].astype(jnp.float32)
                value = (FOUR_PI * own) * partner
                dens[e] = value
                first[e] = value / CHEB_CENTER
                return carry

            lax.fori_loop(0, size, density, 0)

            def sweep_one(e, carry):
                center = first[e]
                remainder = dens[e] - applied(first, e)
                direction = keep_one * center + mix_one * remainder
                rem[e] = remainder
                second[e] = direction
                partial[e] = center + direction
                return carry

            flux[...] = face_z[0] * (first[1] - first[0])
            lax.fori_loop(1, size - 1, sweep_one, 0)

            def sweep_two(e, carry):
                remainder = rem[e] - applied(second, e)
                direction = keep_two * second[e] + mix_two * remainder
                potential = partial[e] + direction
                partner = psi_ref[k + 1, start + e].astype(jnp.float32)
                out_ref[out_at + e - HALO] += (weight * potential) * partner
                return carry

            flux[...] = face_z[1] * (second[2] - second[1])
            lax.fori_loop(HALO, size - HALO, sweep_two, 0)
        out_at += size - 2 * HALO
    out_ref[...] = -out_ref[...]


def solve(weights, psi, eps, windows):
    _, rows, cols = eps.shape
    pairs = psi.shape[0] - 1
    widest = max(size for _, size in windows)
    outputs = sum(size - 2 * HALO for _, size in windows)
    work = sum(3 * size for _, size in windows)
    vmem = pltpu.VMEM
    layer = (rows, cols)
    return pl.pallas_call(
        functools.partial(solve_kernel, tuple(windows)),
        out_shape=jax.ShapeDtypeStruct((outputs,) + layer, jnp.float32),
        in_specs=[pl.BlockSpec(memory_space=vmem)] * 3,
        out_specs=pl.BlockSpec(memory_space=vmem),
        scratch_shapes=[vmem((widest,) + layer, jnp.float32)] * 8 + [vmem(layer, jnp.float32)],
        compiler_params=pltpu.CompilerParams(vmem_limit_bytes=48 * 1024 * 1024),
        cost_estimate=pl.CostEstimate(
            flops=pairs * work * rows * cols * 25,
            transcendentals=0,
            bytes_accessed=psi.size * 2 + eps.size * 4 + outputs * rows * cols * 4,
        ),
    )(weights, psi, eps)


def exchanged(x, axis, pairs_of):
    size = lax.axis_size(axis)
    return lax.ppermute(x, axis, [(i, pairs_of(i) % size) for i in range(size)])


def on_device(orbitals, dielectric, occupied, plan):
    psi = orbitals[0]
    depth, rows, cols = psi.shape
    ticks = plan.shape[0]
    flags = plan.astype(jnp.float32).reshape(ticks)
    padded_diel = z_halo(dielectric, 0, HALO)

    info = jnp.zeros((16, cols), jnp.bfloat16).at[:ticks, :].set(
        jnp.broadcast_to(plan.astype(jnp.bfloat16).reshape(ticks, 1), (ticks, cols))
    )
    message = jnp.concatenate(
        [(psi * occupied.astype(jnp.bfloat16)[0]).reshape(depth * rows, cols), info], axis=0
    )
    swap = exchanged(message, "band", lambda b: b ^ 1)
    outer = exchanged(message, "band", lambda b: b + 1 if b % 2 else b - 1)
    far = exchanged(message, "band", lambda b: b - 2 if b % 2 else b + 2)
    relay = exchanged(outer, "band", lambda b: b ^ 1)

    def slab(m):
        return m[: depth * rows].reshape(depth, rows, cols)

    def sent_flags(m, tick):
        return m[depth * rows + tick : depth * rows + tick + 1].astype(jnp.float32)

    def own_flags(tick):
        return jnp.broadcast_to(flags[tick], (1, cols))

    odd = lax.axis_index("band") % 2 == 1
    weights = jnp.stack(
        [
            jnp.where(odd, own_flags(0), sent_flags(swap, 0)),
            jnp.where(odd, sent_flags(outer, 0), own_flags(0)),
            jnp.where(odd, sent_flags(far, 1), own_flags(1)),
            jnp.where(odd, own_flags(1), sent_flags(relay, 1)),
        ]
    )
    stack = jnp.stack([psi, slab(swap), slab(outer), slab(far), slab(relay)])
    inner = solve(weights, stack, dielectric, [(0, depth)])
    wide = z_halo(stack, 1, HALO)
    edge = solve(weights, wide, padded_diel, [(0, 3 * HALO), (depth - HALO, 3 * HALO)])
    totals = jnp.concatenate([edge[:HALO], inner, edge[HALO:]])
    return totals[None]


def solution(mesh):
    placed = (
        P("band", "depth", None, None),
        P("depth", None, None),
        P("band"),
        P(None, "band", None),
    )
    return jax.shard_map(
        on_device,
        mesh=mesh,
        in_specs=placed,
        out_specs=P("band", "depth", None, None),
        check_vma=False,
    )
```

```python
import functools
import math

import jax
import jax.numpy as jnp
from jax import lax
from jax.experimental import pallas as pl
from jax.experimental.pallas import tpu as pltpu
from jax.sharding import PartitionSpec as P

SWEEPS = 2


FOUR_PI = 4.0 * math.pi
KAPPA_SQ = 4.0
CHEB_CENTER = 28.0
CHEB_HALF = 24.0
HALO = SWEEPS


def shifted(x, axis, by):
    size = lax.axis_size(axis)
    return lax.ppermute(x, axis, [(i, (i + by) % size) for i in range(size)])


def solve_kernel(windows, weight_ref, psi_ref, eps_ref, out_ref, face_z, face_x, face_y, dens, first, rem, second, partial, flux):
    _, rows, cols = eps_ref.shape
    pairs = psi_ref.shape[0] - 1

    def applied(field, e):
        center = field[e]
        flux_up = face_z[e] * (field[e + 1] - center)
        flux_down = flux[...]
        flux[...] = flux_up
        part_z = flux_up - flux_down
        flux_x = face_x[e] * (pltpu.roll(center, rows - 1, 0) - center)
        part_x = flux_x - pltpu.roll(flux_x, 1, 0)
        flux_y = face_y[e] * (pltpu.roll(center, cols - 1, 1) - center)
        part_y = flux_y - pltpu.roll(flux_y, 1, 1)
        return KAPPA_SQ * center - (part_z + part_x + part_y)

    sigma = CHEB_CENTER / CHEB_HALF
    factor = CHEB_HALF / CHEB_CENTER
    factor_one = 1.0 / (2.0 * sigma - factor)
    factor_two = 1.0 / (2.0 * sigma - factor_one)
    keep_one, mix_one = factor_one * factor, 2.0 * factor_one / CHEB_HALF
    keep_two, mix_two = factor_two * factor_one, 2.0 * factor_two / CHEB_HALF

    out_ref[...] = jnp.zeros(out_ref.shape, out_ref.dtype)
    out_at = 0
    for start, size in windows:

        def faces(e, carry):
            cur = eps_ref[start + e]
            face_x[e] = (cur + pltpu.roll(cur, rows - 1, 0)) * 0.5
            face_y[e] = (cur + pltpu.roll(cur, cols - 1, 1)) * 0.5
            face_z[e] = (cur + eps_ref[start + e + 1]) * 0.5
            return carry

        lax.fori_loop(0, size - 1, faces, 0)

        for k in range(pairs):
            weight = weight_ref[k]

            def density(e, carry):
                own = psi_ref[0, start + e].astype(jnp.float32)
                partner = psi_ref[k + 1, start + e].astype(jnp.float32)
                value = (FOUR_PI * own) * partner
                dens[e] = value
                first[e] = value / CHEB_CENTER
                return carry

            lax.fori_loop(0, size, density, 0)

            def sweep_one(e, carry):
                center = first[e]
                remainder = dens[e] - applied(first, e)
                direction = keep_one * center + mix_one * remainder
                rem[e] = remainder
                second[e] = direction
                partial[e] = center + direction
                return carry

            flux[...] = face_z[0] * (first[1] - first[0])
            lax.fori_loop(1, size - 1, sweep_one, 0)

            def sweep_two(e, carry):
                remainder = rem[e] - applied(second, e)
                direction = keep_two * second[e] + mix_two * remainder
                potential = partial[e] + direction
                partner = psi_ref[k + 1, start + e].astype(jnp.float32)
                out_ref[out_at + e - HALO] += (weight * potential) * partner
                return carry

            flux[...] = face_z[1] * (second[2] - second[1])
            lax.fori_loop(HALO, size - HALO, sweep_two, 0)
        out_at += size - 2 * HALO
    out_ref[...] = -out_ref[...]


def solve(weights, psi, eps, windows):
    _, rows, cols = eps.shape
    pairs = psi.shape[0] - 1
    widest = max(size for _, size in windows)
    outputs = sum(size - 2 * HALO for _, size in windows)
    work = sum(3 * size for _, size in windows)
    vmem = pltpu.VMEM
    layer = (rows, cols)
    return pl.pallas_call(
        functools.partial(solve_kernel, tuple(windows)),
        out_shape=jax.ShapeDtypeStruct((outputs,) + layer, jnp.float32),
        in_specs=[pl.BlockSpec(memory_space=vmem)] * 3,
        out_specs=pl.BlockSpec(memory_space=vmem),
        scratch_shapes=[vmem((widest,) + layer, jnp.float32)] * 8 + [vmem(layer, jnp.float32)],
        compiler_params=pltpu.CompilerParams(vmem_limit_bytes=48 * 1024 * 1024),
        cost_estimate=pl.CostEstimate(
            flops=pairs * work * rows * cols * 25,
            transcendentals=0,
            bytes_accessed=psi.size * 2 + eps.size * 4 + outputs * rows * cols * 4,
        ),
    )(weights, psi, eps)


def exchanged(x, axis, pairs_of):
    size = lax.axis_size(axis)
    return lax.ppermute(x, axis, [(i, pairs_of(i) % size) for i in range(size)])


def on_device(orbitals, dielectric, occupied, plan):
    psi = orbitals[0]
    depth, rows, cols = psi.shape
    ticks = plan.shape[0]
    flags = plan.astype(jnp.float32).reshape(ticks)

    info = jnp.zeros((16, cols), jnp.bfloat16).at[:ticks, :].set(
        jnp.broadcast_to(plan.astype(jnp.bfloat16).reshape(ticks, 1), (ticks, cols))
    )
    message = jnp.concatenate(
        [(psi * occupied.astype(jnp.bfloat16)[0]).reshape(depth * rows, cols), info], axis=0
    )
    swap = exchanged(message, "band", lambda b: b ^ 1)
    outer = exchanged(message, "band", lambda b: b + 1 if b % 2 else b - 1)
    far = exchanged(message, "band", lambda b: b - 2 if b % 2 else b + 2)
    relay = exchanged(outer, "band", lambda b: b ^ 1)

    def slab(m):
        return m[: depth * rows].reshape(depth, rows, cols)

    def sent_flags(m, tick):
        return m[depth * rows + tick : depth * rows + tick + 1].astype(jnp.float32)

    def own_flags(tick):
        return jnp.broadcast_to(flags[tick], (1, cols))

    odd = lax.axis_index("band") % 2 == 1
    weights = jnp.stack(
        [
            jnp.where(odd, own_flags(0), sent_flags(swap, 0)),
            jnp.where(odd, sent_flags(outer, 0), own_flags(0)),
            jnp.where(odd, sent_flags(far, 1), own_flags(1)),
            jnp.where(odd, own_flags(1), sent_flags(relay, 1)),
        ]
    )
    stack = jnp.stack([psi, slab(swap), slab(outer), slab(far), slab(relay)])
    inner = solve(weights, stack, dielectric, [(0, depth)])
    lanes = (HALO, rows, cols)
    tops = jnp.concatenate([stack[:, depth - HALO :].astype(jnp.float32).reshape(-1, rows, cols), dielectric[depth - HALO :]])
    bottoms = jnp.concatenate([stack[:, :HALO].astype(jnp.float32).reshape(-1, rows, cols), dielectric[:HALO]])
    with jax.named_scope("halo_up"):
        before = shifted(tops, "depth", 1)
    with jax.named_scope("halo_down"):
        after = shifted(bottoms, "depth", -1)
    slabs = stack.shape[0]

    def orbital_part(h):
        return h[: slabs * HALO].reshape((slabs,) + lanes).astype(jnp.bfloat16)

    wide = jnp.concatenate([orbital_part(before), stack, orbital_part(after)], axis=1)
    padded_diel = jnp.concatenate([before[slabs * HALO :], dielectric, after[slabs * HALO :]])
    edge = solve(weights, wide, padded_diel, [(0, 3 * HALO), (depth - HALO, 3 * HALO)])
    totals = jnp.concatenate([edge[:HALO], inner, edge[HALO:]])
    return totals[None]


def solution(mesh):
    placed = (
        P("band", "depth", None, None),
        P("depth", None, None),
        P("band"),
        P(None, "band", None),
    )
    return jax.shard_map(
        on_device,
        mesh=mesh,
        in_specs=placed,
        out_specs=P("band", "depth", None, None),
        check_vma=False,
    )
```

```python
import functools
import math

import jax
import jax.numpy as jnp
from jax import lax
from jax.experimental import pallas as pl
from jax.experimental.pallas import tpu as pltpu
from jax.sharding import PartitionSpec as P

SWEEPS = 2


FOUR_PI = 4.0 * math.pi
KAPPA_SQ = 4.0
CHEB_CENTER = 28.0
CHEB_HALF = 24.0
HALO = SWEEPS


def shifted(x, axis, by):
    size = lax.axis_size(axis)
    return lax.ppermute(x, axis, [(i, (i + by) % size) for i in range(size)])


def z_halo(x, dim, width):
    length = x.shape[dim]
    last = lax.slice_in_dim(x, length - width, length, axis=dim)
    leading = lax.slice_in_dim(x, 0, width, axis=dim)
    before = shifted(last, "depth", 1)
    after = shifted(leading, "depth", -1)
    return jnp.concatenate([before, x, after], axis=dim)


def solve_kernel(windows, weight_ref, psi_ref, eps_ref, out_ref, face_z, face_x, face_y, dens, first, rem, second, partial, flux):
    _, rows, cols = eps_ref.shape
    pairs = psi_ref.shape[0] - 1

    def applied(field, e):
        center = field[e]
        flux_up = face_z[e] * (field[e + 1] - center)
        flux_down = flux[...]
        flux[...] = flux_up
        part_z = flux_up - flux_down
        flux_x = face_x[e] * (pltpu.roll(center, rows - 1, 0) - center)
        part_x = flux_x - pltpu.roll(flux_x, 1, 0)
        flux_y = face_y[e] * (pltpu.roll(center, cols - 1, 1) - center)
        part_y = flux_y - pltpu.roll(flux_y, 1, 1)
        return KAPPA_SQ * center - (part_z + part_x + part_y)

    sigma = CHEB_CENTER / CHEB_HALF
    factor = CHEB_HALF / CHEB_CENTER
    factor_one = 1.0 / (2.0 * sigma - factor)
    factor_two = 1.0 / (2.0 * sigma - factor_one)
    keep_one, mix_one = factor_one * factor, 2.0 * factor_one / CHEB_HALF
    keep_two, mix_two = factor_two * factor_one, 2.0 * factor_two / CHEB_HALF

    out_ref[...] = jnp.zeros(out_ref.shape, out_ref.dtype)
    out_at = 0
    for start, size in windows:

        def faces(e, carry):
            cur = eps_ref[start + e]
            face_x[e] = (cur + pltpu.roll(cur, rows - 1, 0)) * 0.5
            face_y[e] = (cur + pltpu.roll(cur, cols - 1, 1)) * 0.5
            face_z[e] = (cur + eps_ref[start + e + 1]) * 0.5
            return carry

        lax.fori_loop(0, size - 1, faces, 0)

        for k in range(pairs):
            weight = weight_ref[k]

            def density(e, carry):
                own = psi_ref[0, start + e].astype(jnp.float32)
                partner = psi_ref[k + 1, start + e].astype(jnp.float32)
                value = (FOUR_PI * own) * partner
                dens[e] = value
                first[e] = value / CHEB_CENTER
                return carry

            lax.fori_loop(0, size, density, 0)

            def sweep_one(e, carry):
                center = first[e]
                remainder = dens[e] - applied(first, e)
                direction = keep_one * center + mix_one * remainder
                rem[e] = remainder
                second[e] = direction
                partial[e] = center + direction
                return carry

            flux[...] = face_z[0] * (first[1] - first[0])
            lax.fori_loop(1, size - 1, sweep_one, 0)

            def sweep_two(e, carry):
                remainder = rem[e] - applied(second, e)
                direction = keep_two * second[e] + mix_two * remainder
                potential = partial[e] + direction
                partner = psi_ref[k + 1, start + e].astype(jnp.float32)
                out_ref[out_at + e - HALO] += (weight * potential) * partner
                return carry

            flux[...] = face_z[1] * (second[2] - second[1])
            lax.fori_loop(HALO, size - HALO, sweep_two, 0)
        out_at += size - 2 * HALO
    out_ref[...] = -out_ref[...]


def solve(weights, psi, eps, windows):
    _, rows, cols = eps.shape
    pairs = psi.shape[0] - 1
    widest = max(size for _, size in windows)
    outputs = sum(size - 2 * HALO for _, size in windows)
    work = sum(3 * size for _, size in windows)
    vmem = pltpu.VMEM
    layer = (rows, cols)
    return pl.pallas_call(
        functools.partial(solve_kernel, tuple(windows)),
        out_shape=jax.ShapeDtypeStruct((outputs,) + layer, jnp.float32),
        in_specs=[pl.BlockSpec(memory_space=vmem)] * 3,
        out_specs=pl.BlockSpec(memory_space=vmem),
        scratch_shapes=[vmem((widest,) + layer, jnp.float32)] * 8 + [vmem(layer, jnp.float32)],
        compiler_params=pltpu.CompilerParams(vmem_limit_bytes=48 * 1024 * 1024),
        cost_estimate=pl.CostEstimate(
            flops=pairs * work * rows * cols * 25,
            transcendentals=0,
            bytes_accessed=psi.size * 2 + eps.size * 4 + outputs * rows * cols * 4,
        ),
    )(weights, psi, eps)


def exchanged(x, axis, pairs_of):
    size = lax.axis_size(axis)
    return lax.ppermute(x, axis, [(i, pairs_of(i) % size) for i in range(size)])


def on_device(orbitals, dielectric, occupied, plan):
    psi = orbitals[0]
    depth, rows, cols = psi.shape
    ticks = plan.shape[0]
    flags = plan.astype(jnp.float32).reshape(ticks)
    padded_diel = z_halo(dielectric, 0, HALO)

    info = jnp.zeros((16, cols), jnp.bfloat16).at[:ticks, :].set(
        jnp.broadcast_to(plan.astype(jnp.bfloat16).reshape(ticks, 1), (ticks, cols))
    )
    message = jnp.concatenate(
        [(psi * occupied.astype(jnp.bfloat16)[0]).reshape(depth * rows, cols), info], axis=0
    )
    outer = exchanged(message, "band", lambda b: b + 1 if b % 2 else b - 1)
    far = exchanged(message, "band", lambda b: b - 2 if b % 2 else b + 2)
    both = exchanged(jnp.stack([message, outer]), "band", lambda b: b ^ 1)
    swap, relay = both[0], both[1]

    def slab(m):
        return m[: depth * rows].reshape(depth, rows, cols)

    def sent_flags(m, tick):
        return m[depth * rows + tick : depth * rows + tick + 1].astype(jnp.float32)

    def own_flags(tick):
        return jnp.broadcast_to(flags[tick], (1, cols))

    odd = lax.axis_index("band") % 2 == 1
    weights = jnp.stack(
        [
            jnp.where(odd, own_flags(0), sent_flags(swap, 0)),
            jnp.where(odd, sent_flags(outer, 0), own_flags(0)),
            jnp.where(odd, sent_flags(far, 1), own_flags(1)),
            jnp.where(odd, own_flags(1), sent_flags(relay, 1)),
        ]
    )
    stack = jnp.stack([psi, slab(swap), slab(outer), slab(far), slab(relay)])
    inner = solve(weights, stack, dielectric, [(0, depth)])
    wide = z_halo(stack, 1, HALO)
    edge = solve(weights, wide, padded_diel, [(0, 3 * HALO), (depth - HALO, 3 * HALO)])
    totals = jnp.concatenate([edge[:HALO], inner, edge[HALO:]])
    return totals[None]


def solution(mesh):
    placed = (
        P("band", "depth", None, None),
        P("depth", None, None),
        P("band"),
        P(None, "band", None),
    )
    return jax.shard_map(
        on_device,
        mesh=mesh,
        in_specs=placed,
        out_specs=P("band", "depth", None, None),
        check_vma=False,
    )
```

```python
import functools
import math

import jax
import jax.numpy as jnp
from jax import lax
from jax.experimental import pallas as pl
from jax.experimental.pallas import tpu as pltpu
from jax.sharding import PartitionSpec as P


SWEEPS = 2


FOUR_PI = 4.0 * math.pi
KAPPA_SQ = 4.0
CHEB_CENTER = 28.0
CHEB_HALF = 24.0
HALO = SWEEPS


def shifted(x, axis, by):
    size = lax.axis_size(axis)
    return lax.ppermute(x, axis, [(i, (i + by) % size) for i in range(size)])


def z_halo(x, dim, width):
    length = x.shape[dim]
    last = lax.slice_in_dim(x, length - width, length, axis=dim)
    leading = lax.slice_in_dim(x, 0, width, axis=dim)
    before = shifted(last, "depth", 1)
    after = shifted(leading, "depth", -1)
    return jnp.concatenate([before, x, after], axis=dim)


def solve_kernel(windows, sources, weight_ref, psi_ref, eps_ref, *refs):
    if sources is None:
        middle_ref, out_ref = refs[0], refs[1]
        weights_out = None
        scratch = refs[2:]
    else:
        middle_ref = None
        out_ref, weights_out = refs[0], refs[1]
        scratch = refs[2:]
    face_z, face_x, face_y, dens, first, rem, second, partial, flux = scratch
    _, rows, cols = eps_ref.shape
    pairs = psi_ref.shape[0] - 1

    if sources is not None:
        odd = weight_ref[0]
        for k, (tick, own_when_odd) in enumerate(sources):
            own = weight_ref[1 + tick]
            pick = odd if own_when_odd else 1.0 - odd
            sent = psi_ref[k + 1, pl.ds(sources_row(psi_ref) + tick, 1), :].astype(jnp.float32)
            weights_out[k] = pick * own + (1.0 - pick) * sent
        weight_of = weights_out
    else:
        weight_of = weight_ref

    def layer(slab, e):
        if len(psi_ref.shape) == 4:
            return psi_ref[slab, e].astype(jnp.float32)
        return psi_ref[slab, pl.ds(pl.multiple_of(e * rows, rows), rows), :].astype(jnp.float32)

    def applied(field, e):
        center = field[e]
        flux_up = face_z[e] * (field[e + 1] - center)
        flux_down = flux[...]
        flux[...] = flux_up
        part_z = flux_up - flux_down
        flux_x = face_x[e] * (pltpu.roll(center, rows - 1, 0) - center)
        part_x = flux_x - pltpu.roll(flux_x, 1, 0)
        flux_y = face_y[e] * (pltpu.roll(center, cols - 1, 1) - center)
        part_y = flux_y - pltpu.roll(flux_y, 1, 1)
        return KAPPA_SQ * center - (part_z + part_x + part_y)

    sigma = CHEB_CENTER / CHEB_HALF
    factor = CHEB_HALF / CHEB_CENTER
    factor_one = 1.0 / (2.0 * sigma - factor)
    factor_two = 1.0 / (2.0 * sigma - factor_one)
    keep_one, mix_one = factor_one * factor, 2.0 * factor_one / CHEB_HALF
    keep_two, mix_two = factor_two * factor_one, 2.0 * factor_two / CHEB_HALF

    for start, size, at in windows:
        count = size - 2 * HALO
        out_ref[pl.ds(at, count)] = jnp.zeros((count, rows, cols), out_ref.dtype)

        def faces(e, carry):
            cur = eps_ref[start + e]
            face_x[e] = (cur + pltpu.roll(cur, rows - 1, 0)) * 0.5
            face_y[e] = (cur + pltpu.roll(cur, cols - 1, 1)) * 0.5
            face_z[e] = (cur + eps_ref[start + e + 1]) * 0.5
            return carry

        lax.fori_loop(0, size - 1, faces, 0)

        for k in range(pairs):
            weight = weight_of[k]

            def density(e, carry):
                value = (FOUR_PI * layer(0, start + e)) * layer(k + 1, start + e)
                dens[e] = value
                first[e] = value / CHEB_CENTER
                return carry

            lax.fori_loop(0, size, density, 0)

            def sweep_one(e, carry):
                center = first[e]
                remainder = dens[e] - applied(first, e)
                direction = keep_one * center + mix_one * remainder
                rem[e] = remainder
                second[e] = direction
                partial[e] = center + direction
                return carry

            flux[...] = face_z[0] * (first[1] - first[0])
            lax.fori_loop(1, size - 1, sweep_one, 0)

            def sweep_two(e, carry):
                remainder = rem[e] - applied(second, e)
                direction = keep_two * second[e] + mix_two * remainder
                potential = partial[e] + direction
                out_ref[at + e - HALO] += (weight * potential) * layer(k + 1, start + e)
                return carry

            flux[...] = face_z[1] * (second[2] - second[1])
            lax.fori_loop(HALO, size - HALO, sweep_two, 0)
        out_ref[pl.ds(at, count)] = -out_ref[pl.ds(at, count)]
    if middle_ref is not None:
        out_ref[pl.ds(HALO, middle_ref.shape[0])] = middle_ref[...]


def sources_row(psi_ref):
    return psi_ref.shape[1] - 16


def solve(weights, psi, eps, windows, outputs, sources=None, middle=None):
    _, rows, cols = eps.shape
    pairs = psi.shape[0] - 1
    widest = max(size for _, size, _ in windows)
    work = sum(3 * size for _, size, _ in windows)
    vmem = pltpu.VMEM
    layer = (rows, cols)
    out_shape = [jax.ShapeDtypeStruct((outputs,) + layer, jnp.float32)]
    operands = [weights, psi, eps]
    in_specs = [pl.BlockSpec(memory_space=pltpu.SMEM if sources is not None else vmem), pl.BlockSpec(memory_space=vmem), pl.BlockSpec(memory_space=vmem)]
    if sources is not None:
        out_shape.append(jax.ShapeDtypeStruct((pairs, 1, cols), jnp.float32))
    else:
        operands.append(middle)
        in_specs.append(pl.BlockSpec(memory_space=vmem))
    return pl.pallas_call(
        functools.partial(solve_kernel, tuple(windows), sources),
        out_shape=tuple(out_shape),
        in_specs=in_specs,
        out_specs=tuple(pl.BlockSpec(memory_space=vmem) for _ in out_shape),
        scratch_shapes=[vmem((widest,) + layer, jnp.float32)] * 8 + [vmem(layer, jnp.float32)],
        compiler_params=pltpu.CompilerParams(vmem_limit_bytes=48 * 1024 * 1024),
        cost_estimate=pl.CostEstimate(
            flops=pairs * work * rows * cols * 25,
            transcendentals=0,
            bytes_accessed=psi.size * 2 + eps.size * 4 + outputs * rows * cols * 4,
        ),
    )(*operands)


def exchanged(x, axis, pairs_of):
    size = lax.axis_size(axis)
    return lax.ppermute(x, axis, [(i, pairs_of(i) % size) for i in range(size)])


def on_device(orbitals, dielectric, occupied, plan):
    psi = orbitals[0]
    depth, rows, cols = psi.shape
    ticks = plan.shape[0]
    flags = plan.astype(jnp.float32).reshape(ticks)
    padded_diel = z_halo(dielectric, 0, HALO)

    info = jnp.zeros((16, cols), jnp.bfloat16).at[:ticks, :].set(
        jnp.broadcast_to(plan.astype(jnp.bfloat16).reshape(ticks, 1), (ticks, cols))
    )
    message = jnp.concatenate(
        [(psi * occupied.astype(jnp.bfloat16)[0]).reshape(depth * rows, cols), info], axis=0
    )
    outer = exchanged(message, "band", lambda b: b + 1 if b % 2 else b - 1)
    far = exchanged(message, "band", lambda b: b - 2 if b % 2 else b + 2)
    both = exchanged(jnp.stack([message, outer]), "band", lambda b: b ^ 1)
    swap, relay = both[0], both[1]

    sources = ((0, True), (0, False), (1, False), (1, True))
    odd = (lax.axis_index("band") % 2).astype(jnp.float32)
    scalars = jnp.concatenate([odd[None], flags])
    own = jnp.concatenate([psi.reshape(depth * rows, cols), info], axis=0)
    stack = jnp.stack([own, swap, outer, far, relay])
    inner, weights = solve(scalars, stack, dielectric, [(0, depth, 0)], depth - 2 * HALO, sources=sources)
    layers = stack[:, : depth * rows].reshape(stack.shape[0], depth, rows, cols)
    wide = z_halo(layers, 1, HALO)
    windows = [(0, 3 * HALO, 0), (depth - HALO, 3 * HALO, depth - HALO)]
    (totals,) = solve(weights, wide, padded_diel, windows, depth, middle=inner)
    return totals[None]


def solution(mesh):
    placed = (
        P("band", "depth", None, None),
        P("depth", None, None),
        P("band"),
        P(None, "band", None),
    )

    return jax.shard_map(
        on_device,
        mesh=mesh,
        in_specs=placed,
        out_specs=P("band", "depth", None, None),
        check_vma=False,
    )
```

```python
import functools
import math

import jax
import jax.numpy as jnp
from jax import lax
from jax.experimental import pallas as pl
from jax.experimental.pallas import tpu as pltpu
from jax.sharding import PartitionSpec as P


SWEEPS = 2


FOUR_PI = 4.0 * math.pi
KAPPA_SQ = 4.0
CHEB_CENTER = 28.0
CHEB_HALF = 24.0
HALO = SWEEPS


def shifted(x, axis, by):
    size = lax.axis_size(axis)
    return lax.ppermute(x, axis, [(i, (i + by) % size) for i in range(size)])


def z_halo(x, dim, width):
    length = x.shape[dim]
    last = lax.slice_in_dim(x, length - width, length, axis=dim)
    leading = lax.slice_in_dim(x, 0, width, axis=dim)
    before = shifted(last, "depth", 1)
    after = shifted(leading, "depth", -1)
    return jnp.concatenate([before, x, after], axis=dim)


def solve_kernel(windows, sources, weight_ref, psi_ref, eps_ref, *refs):
    if sources is None:
        middle_ref, kept_second, kept_rem, kept_partial, out_ref = refs[:5]
        weights_out = None
        scratch = refs[5:]
    else:
        middle_ref = None
        out_ref, weights_out, kept_second, kept_rem, kept_partial = refs[:5]
        scratch = refs[5:]
    face_z, face_x, face_y, dens, first, rem, second, partial, flux = scratch
    _, rows, cols = eps_ref.shape
    pairs = psi_ref.shape[0] - 1

    if sources is not None:
        odd = weight_ref[0]
        for k, (tick, own_when_odd) in enumerate(sources):
            own = weight_ref[1 + tick]
            pick = odd if own_when_odd else 1.0 - odd
            sent = psi_ref[k + 1, pl.ds(sources_row(psi_ref) + tick, 1), :].astype(jnp.float32)
            weights_out[k] = pick * own + (1.0 - pick) * sent
        weight_of = weights_out
    else:
        weight_of = weight_ref

    def layer(slab, e):
        if len(psi_ref.shape) == 4:
            return psi_ref[slab, e].astype(jnp.float32)
        return psi_ref[slab, pl.ds(pl.multiple_of(e * rows, rows), rows), :].astype(jnp.float32)

    def applied(field, e):
        center = field[e]
        flux_up = face_z[e] * (field[e + 1] - center)
        flux_down = flux[...]
        flux[...] = flux_up
        part_z = flux_up - flux_down
        flux_x = face_x[e] * (pltpu.roll(center, rows - 1, 0) - center)
        part_x = flux_x - pltpu.roll(flux_x, 1, 0)
        flux_y = face_y[e] * (pltpu.roll(center, cols - 1, 1) - center)
        part_y = flux_y - pltpu.roll(flux_y, 1, 1)
        return KAPPA_SQ * center - (part_z + part_x + part_y)

    sigma = CHEB_CENTER / CHEB_HALF
    factor = CHEB_HALF / CHEB_CENTER
    factor_one = 1.0 / (2.0 * sigma - factor)
    factor_two = 1.0 / (2.0 * sigma - factor_one)
    keep_one, mix_one = factor_one * factor, 2.0 * factor_one / CHEB_HALF
    keep_two, mix_two = factor_two * factor_one, 2.0 * factor_two / CHEB_HALF

    for start, size, at, dens_span, sweep_span, taken in windows:
        count = size - 2 * HALO
        out_ref[pl.ds(at, count)] = jnp.zeros((count, rows, cols), out_ref.dtype)

        def faces(e, carry):
            cur = eps_ref[start + e]
            face_x[e] = (cur + pltpu.roll(cur, rows - 1, 0)) * 0.5
            face_y[e] = (cur + pltpu.roll(cur, cols - 1, 1)) * 0.5
            face_z[e] = (cur + eps_ref[start + e + 1]) * 0.5
            return carry

        lax.fori_loop(0, size - 1, faces, 0)

        for k in range(pairs):
            weight = weight_of[k]

            def density(e, carry):
                value = (FOUR_PI * layer(0, start + e)) * layer(k + 1, start + e)
                dens[e] = value
                first[e] = value / CHEB_CENTER
                return carry

            lax.fori_loop(dens_span[0], dens_span[1], density, 0)

            def sweep_one(e, carry):
                center = first[e]
                remainder = dens[e] - applied(first, e)
                direction = keep_one * center + mix_one * remainder
                rem[e] = remainder
                second[e] = direction
                partial[e] = center + direction
                return carry

            lo, hi = sweep_span
            flux[...] = face_z[lo - 1] * (first[lo] - first[lo - 1])
            lax.fori_loop(lo, hi, sweep_one, 0)
            if sources is not None:
                for j, e in enumerate((1, 2, size - 3, size - 2)):
                    kept_second[k, j] = second[e]
                for j, e in enumerate((1, size - 2)):
                    kept_rem[k, j] = rem[e]
                    kept_partial[k, j] = partial[e]
            else:
                seconds, both = taken
                for e, j in seconds:
                    second[e] = kept_second[k, j]
                e, j = both
                rem[e] = kept_rem[k, j]
                partial[e] = kept_partial[k, j]

            def sweep_two(e, carry):
                remainder = rem[e] - applied(second, e)
                direction = keep_two * second[e] + mix_two * remainder
                potential = partial[e] + direction
                out_ref[at + e - HALO] += (weight * potential) * layer(k + 1, start + e)
                return carry

            flux[...] = face_z[1] * (second[2] - second[1])
            lax.fori_loop(HALO, size - HALO, sweep_two, 0)
        out_ref[pl.ds(at, count)] = -out_ref[pl.ds(at, count)]
    if middle_ref is not None:
        out_ref[pl.ds(HALO, middle_ref.shape[0])] = middle_ref[...]


def sources_row(psi_ref):
    return psi_ref.shape[1] - 16


def solve(weights, psi, eps, windows, outputs, sources=None, middle=None, kept=None):
    rows, cols = eps.shape[1:]
    pairs = psi.shape[0] - 1
    widest = max(window[1] for window in windows)
    work = sum(3 * window[1] for window in windows)
    vmem = pltpu.VMEM
    layer = (rows, cols)
    kept_shapes = [
        jax.ShapeDtypeStruct((pairs, 4) + layer, jnp.float32),
        jax.ShapeDtypeStruct((pairs, 2) + layer, jnp.float32),
        jax.ShapeDtypeStruct((pairs, 2) + layer, jnp.float32),
    ]
    out_shape = [jax.ShapeDtypeStruct((outputs,) + layer, jnp.float32)]
    operands = [weights, psi, eps]
    in_specs = [pl.BlockSpec(memory_space=pltpu.SMEM if sources is not None else vmem), pl.BlockSpec(memory_space=vmem), pl.BlockSpec(memory_space=vmem)]
    if sources is not None:
        out_shape += [jax.ShapeDtypeStruct((pairs, 1, cols), jnp.float32)] + kept_shapes
    else:
        operands += [middle] + list(kept)
        in_specs += [pl.BlockSpec(memory_space=vmem)] * 4
    return pl.pallas_call(
        functools.partial(solve_kernel, tuple(windows), sources),
        out_shape=tuple(out_shape),
        in_specs=in_specs,
        out_specs=tuple(pl.BlockSpec(memory_space=vmem) for _ in out_shape),
        scratch_shapes=[vmem((widest,) + layer, jnp.float32)] * 8 + [vmem(layer, jnp.float32)],
        compiler_params=pltpu.CompilerParams(vmem_limit_bytes=48 * 1024 * 1024),
        cost_estimate=pl.CostEstimate(
            flops=pairs * work * rows * cols * 25,
            transcendentals=0,
            bytes_accessed=psi.size * 2 + eps.size * 4 + outputs * rows * cols * 4,
        ),
    )(*operands)


def exchanged(x, axis, pairs_of):
    size = lax.axis_size(axis)
    return lax.ppermute(x, axis, [(i, pairs_of(i) % size) for i in range(size)])


def on_device(orbitals, dielectric, occupied, plan):
    psi = orbitals[0]
    depth, rows, cols = psi.shape
    ticks = plan.shape[0]
    flags = plan.astype(jnp.float32).reshape(ticks)
    padded_diel = z_halo(dielectric, 0, HALO)

    info = jnp.zeros((16, cols), jnp.bfloat16).at[:ticks, :].set(
        jnp.broadcast_to(plan.astype(jnp.bfloat16).reshape(ticks, 1), (ticks, cols))
    )
    message = jnp.concatenate(
        [(psi * occupied.astype(jnp.bfloat16)[0]).reshape(depth * rows, cols), info], axis=0
    )
    outer = exchanged(message, "band", lambda b: b + 1 if b % 2 else b - 1)
    far = exchanged(message, "band", lambda b: b - 2 if b % 2 else b + 2)
    both = exchanged(jnp.stack([message, outer]), "band", lambda b: b ^ 1)
    swap, relay = both[0], both[1]

    sources = ((0, True), (0, False), (1, False), (1, True))
    odd = (lax.axis_index("band") % 2).astype(jnp.float32)
    scalars = jnp.concatenate([odd[None], flags])
    own = jnp.concatenate([psi.reshape(depth * rows, cols), info], axis=0)
    stack = jnp.stack([own, swap, outer, far, relay])
    inner, weights, *kept = solve(
        scalars, stack, dielectric, [(0, depth, 0, (0, depth), (1, depth - 1), None)], depth - 2 * HALO, sources=sources
    )
    layers = stack[:, : depth * rows].reshape(stack.shape[0], depth, rows, cols)
    wide = z_halo(layers, 1, HALO)
    windows = [
        (0, 3 * HALO, 0, (0, 4), (1, 3), (((3, 0), (4, 1)), (3, 0))),
        (depth - HALO, 3 * HALO, depth - HALO, (2, 6), (3, 5), (((1, 2), (2, 3)), (2, 1))),
    ]
    (totals,) = solve(weights, wide, padded_diel, windows, depth, middle=inner, kept=kept)
    return totals[None]


def solution(mesh):
    placed = (
        P("band", "depth", None, None),
        P("depth", None, None),
        P("band"),
        P(None, "band", None),
    )

    return jax.shard_map(
        on_device,
        mesh=mesh,
        in_specs=placed,
        out_specs=P("band", "depth", None, None),
        check_vma=False,
    )
```

```python
import functools
import math

import jax
import jax.numpy as jnp
from jax import lax
from jax.experimental import pallas as pl
from jax.experimental.pallas import tpu as pltpu
from jax.sharding import PartitionSpec as P


SWEEPS = 2


FOUR_PI = 4.0 * math.pi
KAPPA_SQ = 4.0
CHEB_CENTER = 28.0
CHEB_HALF = 24.0
HALO = SWEEPS


def shifted(x, axis, by):
    size = lax.axis_size(axis)
    return lax.ppermute(x, axis, [(i, (i + by) % size) for i in range(size)])


def z_halo(x, dim, width):
    length = x.shape[dim]
    last = lax.slice_in_dim(x, length - width, length, axis=dim)
    leading = lax.slice_in_dim(x, 0, width, axis=dim)
    before = shifted(last, "depth", 1)
    after = shifted(leading, "depth", -1)
    return jnp.concatenate([before, x, after], axis=dim)


def solve_kernel(windows, sources, weight_ref, psi_ref, eps_ref, *refs):
    if sources is None:
        middle_ref, kept_second, kept_rem, kept_partial, out_ref = refs[:5]
        weights_out = None
        scratch = refs[5:]
    else:
        middle_ref = None
        out_ref, weights_out, kept_second, kept_rem, kept_partial = refs[:5]
        scratch = refs[5:]
    face_z, face_x, face_y, dens, first, rem, second, partial, flux = scratch
    _, rows, cols = eps_ref.shape
    pairs = psi_ref.shape[0] - 1

    if sources is not None:
        odd = weight_ref[0]
        for k, (tick, own_when_odd) in enumerate(sources):
            own = weight_ref[1 + tick]
            pick = odd if own_when_odd else 1.0 - odd
            sent = psi_ref[k + 1, pl.ds(sources_row(psi_ref) + tick, 1), :].astype(jnp.float32)
            weights_out[k] = pick * own + (1.0 - pick) * sent
        weight_of = weights_out
    else:
        weight_of = weight_ref

    def layer(slab, e):
        if len(psi_ref.shape) == 4:
            return psi_ref[slab, e].astype(jnp.float32)
        return psi_ref[slab, pl.ds(pl.multiple_of(e * rows, rows), rows), :].astype(jnp.float32)

    def applied(field, e):
        center = field[e]
        flux_up = face_z[e] * (field[e + 1] - center)
        flux_down = flux[...]
        flux[...] = flux_up
        part_z = flux_up - flux_down
        flux_x = face_x[e] * (pltpu.roll(center, rows - 1, 0) - center)
        part_x = flux_x - pltpu.roll(flux_x, 1, 0)
        flux_y = face_y[e] * (pltpu.roll(center, cols - 1, 1) - center)
        part_y = flux_y - pltpu.roll(flux_y, 1, 1)
        return KAPPA_SQ * center - (part_z + part_x + part_y)

    sigma = CHEB_CENTER / CHEB_HALF
    factor = CHEB_HALF / CHEB_CENTER
    factor_one = 1.0 / (2.0 * sigma - factor)
    factor_two = 1.0 / (2.0 * sigma - factor_one)
    keep_one, mix_one = factor_one * factor, 2.0 * factor_one / CHEB_HALF
    keep_two, mix_two = factor_two * factor_one, 2.0 * factor_two / CHEB_HALF

    for start, size, at, dens_span, sweep_span, taken in windows:
        count = size - 2 * HALO
        out_ref[pl.ds(at, count)] = jnp.zeros((count, rows, cols), out_ref.dtype)

        def faces(e, carry):
            cur = eps_ref[start + e]
            face_x[e] = (cur + pltpu.roll(cur, rows - 1, 0)) * 0.5
            face_y[e] = (cur + pltpu.roll(cur, cols - 1, 1)) * 0.5
            face_z[e] = (cur + eps_ref[start + e + 1]) * 0.5
            return carry

        lax.fori_loop(0, size - 1, faces, 0, unroll=True)

        for k in range(pairs):
            weight = weight_of[k]

            def density(e, carry):
                value = (FOUR_PI * layer(0, start + e)) * layer(k + 1, start + e)
                dens[e] = value
                first[e] = value / CHEB_CENTER
                return carry

            lax.fori_loop(dens_span[0], dens_span[1], density, 0, unroll=True)

            def sweep_one(e, carry):
                center = first[e]
                remainder = dens[e] - applied(first, e)
                direction = keep_one * center + mix_one * remainder
                rem[e] = remainder
                second[e] = direction
                partial[e] = center + direction
                return carry

            lo, hi = sweep_span
            flux[...] = face_z[lo - 1] * (first[lo] - first[lo - 1])
            lax.fori_loop(lo, hi, sweep_one, 0, unroll=2)
            if sources is not None:
                for j, e in enumerate((1, 2, size - 3, size - 2)):
                    kept_second[k, j] = second[e]
                for j, e in enumerate((1, size - 2)):
                    kept_rem[k, j] = rem[e]
                    kept_partial[k, j] = partial[e]
            else:
                seconds, both = taken
                for e, j in seconds:
                    second[e] = kept_second[k, j]
                e, j = both
                rem[e] = kept_rem[k, j]
                partial[e] = kept_partial[k, j]

            def sweep_two(e, carry):
                remainder = rem[e] - applied(second, e)
                direction = keep_two * second[e] + mix_two * remainder
                potential = partial[e] + direction
                out_ref[at + e - HALO] += (weight * potential) * layer(k + 1, start + e)
                return carry

            flux[...] = face_z[1] * (second[2] - second[1])
            lax.fori_loop(HALO, size - HALO, sweep_two, 0, unroll=2)
        out_ref[pl.ds(at, count)] = -out_ref[pl.ds(at, count)]
    if middle_ref is not None:
        out_ref[pl.ds(HALO, middle_ref.shape[0])] = middle_ref[...]


def sources_row(psi_ref):
    return psi_ref.shape[1] - 16


def solve(weights, psi, eps, windows, outputs, sources=None, middle=None, kept=None):
    rows, cols = eps.shape[1:]
    pairs = psi.shape[0] - 1
    widest = max(window[1] for window in windows)
    work = sum(3 * window[1] for window in windows)
    vmem = pltpu.VMEM
    layer = (rows, cols)
    kept_shapes = [
        jax.ShapeDtypeStruct((pairs, 4) + layer, jnp.float32),
        jax.ShapeDtypeStruct((pairs, 2) + layer, jnp.float32),
        jax.ShapeDtypeStruct((pairs, 2) + layer, jnp.float32),
    ]
    out_shape = [jax.ShapeDtypeStruct((outputs,) + layer, jnp.float32)]
    operands = [weights, psi, eps]
    in_specs = [pl.BlockSpec(memory_space=pltpu.SMEM if sources is not None else vmem), pl.BlockSpec(memory_space=vmem), pl.BlockSpec(memory_space=vmem)]
    if sources is not None:
        out_shape += [jax.ShapeDtypeStruct((pairs, 1, cols), jnp.float32)] + kept_shapes
    else:
        operands += [middle] + list(kept)
        in_specs += [pl.BlockSpec(memory_space=vmem)] * 4
    return pl.pallas_call(
        functools.partial(solve_kernel, tuple(windows), sources),
        out_shape=tuple(out_shape),
        in_specs=in_specs,
        out_specs=tuple(pl.BlockSpec(memory_space=vmem) for _ in out_shape),
        scratch_shapes=[vmem((widest,) + layer, jnp.float32)] * 8 + [vmem(layer, jnp.float32)],
        compiler_params=pltpu.CompilerParams(vmem_limit_bytes=48 * 1024 * 1024),
        cost_estimate=pl.CostEstimate(
            flops=pairs * work * rows * cols * 25,
            transcendentals=0,
            bytes_accessed=psi.size * 2 + eps.size * 4 + outputs * rows * cols * 4,
        ),
    )(*operands)


def exchanged(x, axis, pairs_of):
    size = lax.axis_size(axis)
    return lax.ppermute(x, axis, [(i, pairs_of(i) % size) for i in range(size)])


def on_device(orbitals, dielectric, occupied, plan):
    psi = orbitals[0]
    depth, rows, cols = psi.shape
    ticks = plan.shape[0]
    flags = plan.astype(jnp.float32).reshape(ticks)
    padded_diel = z_halo(dielectric, 0, HALO)

    info = jnp.zeros((16, cols), jnp.bfloat16).at[:ticks, :].set(
        jnp.broadcast_to(plan.astype(jnp.bfloat16).reshape(ticks, 1), (ticks, cols))
    )
    message = jnp.concatenate(
        [(psi * occupied.astype(jnp.bfloat16)[0]).reshape(depth * rows, cols), info], axis=0
    )
    outer = exchanged(message, "band", lambda b: b + 1 if b % 2 else b - 1)
    far = exchanged(message, "band", lambda b: b - 2 if b % 2 else b + 2)
    both = exchanged(jnp.stack([message, outer]), "band", lambda b: b ^ 1)
    swap, relay = both[0], both[1]

    sources = ((0, True), (0, False), (1, False), (1, True))
    odd = (lax.axis_index("band") % 2).astype(jnp.float32)
    scalars = jnp.concatenate([odd[None], flags])
    own = jnp.concatenate([psi.reshape(depth * rows, cols), info], axis=0)
    stack = jnp.stack([own, swap, outer, far, relay])
    inner, weights, *kept = solve(
        scalars, stack, dielectric, [(0, depth, 0, (0, depth), (1, depth - 1), None)], depth - 2 * HALO, sources=sources
    )
    layers = stack[:, : depth * rows].reshape(stack.shape[0], depth, rows, cols)
    wide = z_halo(layers, 1, HALO)
    windows = [
        (0, 3 * HALO, 0, (0, 4), (1, 3), (((3, 0), (4, 1)), (3, 0))),
        (depth - HALO, 3 * HALO, depth - HALO, (2, 6), (3, 5), (((1, 2), (2, 3)), (2, 1))),
    ]
    (totals,) = solve(weights, wide, padded_diel, windows, depth, middle=inner, kept=kept)
    return totals[None]


def solution(mesh):
    placed = (
        P("band", "depth", None, None),
        P("depth", None, None),
        P("band"),
        P(None, "band", None),
    )

    return jax.shard_map(
        on_device,
        mesh=mesh,
        in_specs=placed,
        out_specs=P("band", "depth", None, None),
        check_vma=False,
    )
```

```python
import functools
import math

import jax
import jax.numpy as jnp
from jax import lax
from jax.experimental import pallas as pl
from jax.experimental.pallas import tpu as pltpu
from jax.sharding import PartitionSpec as P


SWEEPS = 2


FOUR_PI = 4.0 * math.pi
KAPPA_SQ = 4.0
CHEB_CENTER = 28.0
CHEB_HALF = 24.0
HALO = SWEEPS


def shifted(x, axis, by):
    size = lax.axis_size(axis)
    return lax.ppermute(x, axis, [(i, (i + by) % size) for i in range(size)])


def z_halo(x, dim, width):
    length = x.shape[dim]
    last = lax.slice_in_dim(x, length - width, length, axis=dim)
    leading = lax.slice_in_dim(x, 0, width, axis=dim)
    before = shifted(last, "depth", 1)
    after = shifted(leading, "depth", -1)
    return jnp.concatenate([before, x, after], axis=dim)


def solve_kernel(windows, sources, weight_ref, psi_ref, eps_ref, *refs):
    if sources is None:
        middle_ref, kept_second, kept_rem, kept_partial, out_ref = refs[:5]
        weights_out = None
        scratch = refs[5:]
    else:
        middle_ref = None
        out_ref, weights_out, kept_second, kept_rem, kept_partial = refs[:5]
        scratch = refs[5:]
    face_z, face_x, face_y, dens, first, rem, second, partial, flux = scratch
    _, rows, cols = eps_ref.shape
    pairs = psi_ref.shape[0] - 1

    if sources is not None:
        odd = weight_ref[0]
        for k, (tick, own_when_odd) in enumerate(sources):
            own = weight_ref[1 + tick]
            pick = odd if own_when_odd else 1.0 - odd
            sent = psi_ref[k + 1, pl.ds(sources_row(psi_ref) + tick, 1), :].astype(jnp.float32)
            weights_out[k] = pick * own + (1.0 - pick) * sent
        weight_of = weights_out
    else:
        weight_of = weight_ref

    def layer(slab, e):
        if len(psi_ref.shape) == 4:
            return psi_ref[slab, e].astype(jnp.float32)
        return psi_ref[slab, pl.ds(pl.multiple_of(e * rows, rows), rows), :].astype(jnp.float32)

    def applied(field, e):
        center = field[e]
        flux_up = face_z[e] * (field[e + 1] - center)
        flux_down = flux[...]
        flux[...] = flux_up
        part_z = flux_up - flux_down
        flux_x = face_x[e] * (pltpu.roll(center, rows - 1, 0) - center)
        part_x = flux_x - pltpu.roll(flux_x, 1, 0)
        flux_y = face_y[e] * (pltpu.roll(center, cols - 1, 1) - center)
        part_y = flux_y - pltpu.roll(flux_y, 1, 1)
        return KAPPA_SQ * center - (part_z + part_x + part_y)

    sigma = CHEB_CENTER / CHEB_HALF
    factor = CHEB_HALF / CHEB_CENTER
    factor_one = 1.0 / (2.0 * sigma - factor)
    factor_two = 1.0 / (2.0 * sigma - factor_one)
    keep_one, mix_one = factor_one * factor, 2.0 * factor_one / CHEB_HALF
    keep_two, mix_two = factor_two * factor_one, 2.0 * factor_two / CHEB_HALF

    for start, size, at, dens_span, sweep_span, taken in windows:
        count = size - 2 * HALO
        out_ref[pl.ds(at, count)] = jnp.zeros((count, rows, cols), out_ref.dtype)

        def faces(e, carry):
            cur = eps_ref[start + e]
            face_x[e] = (cur + pltpu.roll(cur, rows - 1, 0)) * 0.5
            face_y[e] = (cur + pltpu.roll(cur, cols - 1, 1)) * 0.5
            face_z[e] = (cur + eps_ref[start + e + 1]) * 0.5
            return carry

        lax.fori_loop(0, size - 1, faces, 0, unroll=True)

        for k in range(pairs):
            weight = weight_of[k]

            def density(e, carry):
                value = (FOUR_PI * layer(0, start + e)) * layer(k + 1, start + e)
                dens[e] = value
                first[e] = value / CHEB_CENTER
                return carry

            lax.fori_loop(dens_span[0], dens_span[1], density, 0, unroll=2)

            def sweep_one(e, carry):
                center = first[e]
                remainder = dens[e] - applied(first, e)
                direction = keep_one * center + mix_one * remainder
                rem[e] = remainder
                second[e] = direction
                partial[e] = center + direction
                return carry

            lo, hi = sweep_span
            flux[...] = face_z[lo - 1] * (first[lo] - first[lo - 1])
            lax.fori_loop(lo, hi, sweep_one, 0, unroll=True)
            if sources is not None:
                for j, e in enumerate((1, 2, size - 3, size - 2)):
                    kept_second[k, j] = second[e]
                for j, e in enumerate((1, size - 2)):
                    kept_rem[k, j] = rem[e]
                    kept_partial[k, j] = partial[e]
            else:
                seconds, both = taken
                for e, j in seconds:
                    second[e] = kept_second[k, j]
                e, j = both
                rem[e] = kept_rem[k, j]
                partial[e] = kept_partial[k, j]

            def sweep_two(e, carry):
                remainder = rem[e] - applied(second, e)
                direction = keep_two * second[e] + mix_two * remainder
                potential = partial[e] + direction
                out_ref[at + e - HALO] += (weight * potential) * layer(k + 1, start + e)
                return carry

            flux[...] = face_z[1] * (second[2] - second[1])
            lax.fori_loop(HALO, size - HALO, sweep_two, 0, unroll=True)
        out_ref[pl.ds(at, count)] = -out_ref[pl.ds(at, count)]
    if middle_ref is not None:
        out_ref[pl.ds(HALO, middle_ref.shape[0])] = middle_ref[...]


def sources_row(psi_ref):
    return psi_ref.shape[1] - 16


def solve(weights, psi, eps, windows, outputs, sources=None, middle=None, kept=None):
    rows, cols = eps.shape[1:]
    pairs = psi.shape[0] - 1
    widest = max(window[1] for window in windows)
    work = sum(3 * window[1] for window in windows)
    vmem = pltpu.VMEM
    layer = (rows, cols)
    kept_shapes = [
        jax.ShapeDtypeStruct((pairs, 4) + layer, jnp.float32),
        jax.ShapeDtypeStruct((pairs, 2) + layer, jnp.float32),
        jax.ShapeDtypeStruct((pairs, 2) + layer, jnp.float32),
    ]
    out_shape = [jax.ShapeDtypeStruct((outputs,) + layer, jnp.float32)]
    operands = [weights, psi, eps]
    in_specs = [pl.BlockSpec(memory_space=pltpu.SMEM if sources is not None else vmem), pl.BlockSpec(memory_space=vmem), pl.BlockSpec(memory_space=vmem)]
    if sources is not None:
        out_shape += [jax.ShapeDtypeStruct((pairs, 1, cols), jnp.float32)] + kept_shapes
    else:
        operands += [middle] + list(kept)
        in_specs += [pl.BlockSpec(memory_space=vmem)] * 4
    return pl.pallas_call(
        functools.partial(solve_kernel, tuple(windows), sources),
        out_shape=tuple(out_shape),
        in_specs=in_specs,
        out_specs=tuple(pl.BlockSpec(memory_space=vmem) for _ in out_shape),
        scratch_shapes=[vmem((widest,) + layer, jnp.float32)] * 8 + [vmem(layer, jnp.float32)],
        compiler_params=pltpu.CompilerParams(vmem_limit_bytes=48 * 1024 * 1024),
        cost_estimate=pl.CostEstimate(
            flops=pairs * work * rows * cols * 25,
            transcendentals=0,
            bytes_accessed=psi.size * 2 + eps.size * 4 + outputs * rows * cols * 4,
        ),
    )(*operands)


def exchanged(x, axis, pairs_of):
    size = lax.axis_size(axis)
    return lax.ppermute(x, axis, [(i, pairs_of(i) % size) for i in range(size)])


def on_device(orbitals, dielectric, occupied, plan):
    psi = orbitals[0]
    depth, rows, cols = psi.shape
    ticks = plan.shape[0]
    flags = plan.astype(jnp.float32).reshape(ticks)
    padded_diel = z_halo(dielectric, 0, HALO)

    info = jnp.zeros((16, cols), jnp.bfloat16).at[:ticks, :].set(
        jnp.broadcast_to(plan.astype(jnp.bfloat16).reshape(ticks, 1), (ticks, cols))
    )
    message = jnp.concatenate(
        [(psi * occupied.astype(jnp.bfloat16)[0]).reshape(depth * rows, cols), info], axis=0
    )
    outer = exchanged(message, "band", lambda b: b + 1 if b % 2 else b - 1)
    far = exchanged(message, "band", lambda b: b - 2 if b % 2 else b + 2)
    both = exchanged(jnp.stack([message, outer]), "band", lambda b: b ^ 1)
    swap, relay = both[0], both[1]

    sources = ((0, True), (0, False), (1, False), (1, True))
    odd = (lax.axis_index("band") % 2).astype(jnp.float32)
    scalars = jnp.concatenate([odd[None], flags])
    own = jnp.concatenate([psi.reshape(depth * rows, cols), info], axis=0)
    stack = jnp.stack([own, swap, outer, far, relay])
    inner, weights, *kept = solve(
        scalars, stack, dielectric, [(0, depth, 0, (0, depth), (1, depth - 1), None)], depth - 2 * HALO, sources=sources
    )
    layers = stack[:, : depth * rows].reshape(stack.shape[0], depth, rows, cols)
    wide = z_halo(layers, 1, HALO)
    windows = [
        (0, 3 * HALO, 0, (0, 4), (1, 3), (((3, 0), (4, 1)), (3, 0))),
        (depth - HALO, 3 * HALO, depth - HALO, (2, 6), (3, 5), (((1, 2), (2, 3)), (2, 1))),
    ]
    (totals,) = solve(weights, wide, padded_diel, windows, depth, middle=inner, kept=kept)
    return totals[None]


def solution(mesh):
    placed = (
        P("band", "depth", None, None),
        P("depth", None, None),
        P("band"),
        P(None, "band", None),
    )

    return jax.shard_map(
        on_device,
        mesh=mesh,
        in_specs=placed,
        out_specs=P("band", "depth", None, None),
        check_vma=False,
    )
```
